128 devices in a mesh: lead: 32 (over x, y_lo, z), sub: 4 (over y_hi, core).
Axes of the slice: x: 4, y: 4 (y_hi: 2, y_lo: 2; y = y_hi * 2 + y_lo), z: 4, core: 2. Of those that a mesh axis runs over, the one named last changes fastest.
Arguments:
- state: float32 [67108864], P(('lead', 'sub')), may hold values from 0.135 to 67, as said below
- couplings: float32 [2, 16], replicated, may hold values from 0.25 to 16, as said below
Outputs:
- evolved: float32 [67108864], P(('lead', 'sub'))
- log_growth: float32 [], replicated
The draws below stay inside these ranges and needn't reach their ends.
Inputs may be any that keep to these rules, and one draw needn't show every extreme that they name: `state`: every entry is positive. `couplings`: row 0 lies between 8 and 16, row 1 between 0.25 and 0.5.
All inputs are finite; a program needn't handle non-finite values.
Results may differ from the reference program's by a relative error of at most 0.0003.
Values sent between devices are 32-bit elements; how exact they have to be, the bound alone decides.
No kernel may reach another device: no remote copies, remote signals or barrier semaphores. Data moves between devices by JAX's collectives and lax.ppermute only.
A program may use at most 64 MiB of HBM per device.

```python
import jax
import jax.numpy as jnp
from jax import lax

W = 13
BLOCK = 4
WINDOWS = 2
SITES = 16


def draw_state(key, part):
    position = jnp.arange(4 ** W, dtype=jnp.int32)
    period = 4 ** (W - 2 * BLOCK)
    fraction = (position % period).astype(jnp.float32) / period
    jitter = jnp.clip(0.8 * jax.random.normal(key, (4 ** W,), jnp.float32), -2.0, 2.0)
    ramp_up = 1.0 + 4.0 * fraction
    return jnp.exp(jitter) * ramp_up


def draw_couplings(key, part):
    vertical_key = jax.random.fold_in(key, 11)
    horizontal_key = jax.random.fold_in(key, 23)
    vertical = jax.random.uniform(vertical_key, (SITES,), jnp.float32, 8.0, 16.0)
    horizontal = jax.random.uniform(horizontal_key, (SITES,), jnp.float32, 0.25, 0.5)
    return jnp.stack([vertical, horizontal])


def setup_inputs(seed: int = 0) -> dict:
    streams_of = jax.random.split(jax.random.key(seed), 3)
    state = draw_state(jax.random.fold_in(streams_of[2], 71), 0)
    couplings = draw_couplings(jax.random.fold_in(streams_of[2], 71), 0)
    return {"state": state, "couplings": couplings}


def one_site(field, vertical, horizontal):
    middle = field.shape[0] // 16
    shaped = field.reshape(4, middle, 4)
    summed = jnp.sum(shaped, axis=0)
    labels = jnp.arange(4, dtype=jnp.int32)

    def column(spin_value):
        spin_row = lax.dynamic_index_in_dim(shaped, spin_value, 0, keepdims=False)
        same_spin = (labels == spin_value).astype(field.dtype)
        return (summed + vertical * spin_row) * (1.0 + horizontal * same_spin)[None, :]

    columns = lax.map(column, labels)
    return jnp.transpose(columns, (1, 2, 0)).reshape(-1)


def reference(state, couplings):
    field_now = state
    growth = jnp.zeros((), state.dtype)
    for window in range(WINDOWS):
        for site_step in range(2 * BLOCK):
            site_index = window * 2 * BLOCK + site_step
            field_now = one_site(field_now, couplings[0, site_index], couplings[1, site_index])
        mean_value = jnp.sum(field_now) / field_now.shape[0]
        field_now = field_now / mean_value
        growth = growth + jnp.log(mean_value)
    return field_now, growth
```

```python
import jax
import jax.numpy as jnp
from jax import lax
from jax.sharding import PartitionSpec as P

BLOCK = 4
WINDOWS = 2
AXES = ("lead", "sub")


def block_kernel(vertical, horizontal, spread):
    position = jnp.arange(spread, dtype=jnp.int32)
    digits = [position // 4 ** (BLOCK - 1 - level) % 4 for level in range(BLOCK)]
    kernel = jnp.ones((spread, spread), jnp.float32)
    for level in range(BLOCK):
        same_spin = (digits[level][:, None] == digits[level][None, :]).astype(jnp.float32)
        kernel = kernel * (1.0 + vertical[level] * same_spin)
    for level in range(1, BLOCK):
        chained = (digits[level - 1] == digits[level]).astype(jnp.float32)
        kernel = kernel * (1.0 + horizontal[level] * chained)[None, :]
    labels = jnp.arange(4, dtype=jnp.int32)
    first_bond = 1.0 + horizontal[0] * (labels[:, None] == labels[None, :]).astype(jnp.float32)
    return (kernel, first_bond)


def multiply(matrix, kernel):
    return lax.dot_general(
        matrix,
        kernel,
        (((0,), (0,)), ((), ())),
        precision=lax.Precision.HIGHEST,
        preferred_element_type=jnp.float32,
    )


def contract(flat, kernel, first_bond, spread):
    result = multiply(flat.reshape(spread, -1), kernel)
    bonded = result.reshape(-1, 4, 4, spread // 4) * first_bond[None, :, :, None]
    return bonded.reshape(-1)


def exchange(flat, devices, minor, extra=None):
    shaped = flat.reshape(-1, devices, minor)
    rows = jnp.transpose(shaped, (1, 0, 2)).reshape(devices, -1)
    if extra is not None:
        rows = jnp.concatenate([rows, extra], axis=1)
    return lax.all_to_all(rows, AXES, 0, 0, tiled=True)


def shards(state, couplings):
    lead_count = lax.axis_size("lead")
    sub_count = lax.axis_size("sub")
    devices = lead_count * sub_count
    me = lax.axis_index("lead") * sub_count + lax.axis_index("sub")
    spread = 4**BLOCK
    whole_count = state.shape[0] * devices
    minor = 4**5 // devices
    kernels = []
    for block in range(2 * WINDOWS):
        first_site = block * BLOCK
        kernels.append(
            block_kernel(
                couplings[0, first_site : first_site + BLOCK],
                couplings[1, first_site : first_site + BLOCK],
                spread,
            )
        )

    current = exchange(state, devices, minor).reshape(-1)
    current = contract(current, *kernels[0], spread)
    current = contract(current, *kernels[1], spread)

    kernel3, bond3 = kernels[2]
    kernel4, bond4 = kernels[3]
    tail = kernel4.reshape(spread, 4, spread // 4).sum(axis=2)
    tail = lax.dot_general(tail, bond4, (((1,), (1,)), ((), ())), precision=lax.Precision.HIGHEST)
    column = jnp.arange(spread, dtype=jnp.int32)
    gather = bond3[:, column // (spread // 4)].T[:, None, :] * tail[:, column % 4].T[:, :, None]
    per_row = spread // devices
    rows = lax.dynamic_slice_in_dim(kernel3, me * per_row, per_row, axis=0)
    weight = lax.dot_general(
        rows, gather.reshape(spread, -1), (((1,), (0,)), ((), ())), precision=lax.Precision.HIGHEST
    ).reshape(per_row, spread, 1, 4)
    middle_part = jnp.sum(current)
    final_part = jnp.sum(current.reshape(per_row, spread, -1, 4) * weight)

    extra = jnp.zeros((devices, 128), jnp.float32)
    extra = extra.at[:, 0].set(middle_part).at[:, 1].set(final_part)
    received = exchange(current, devices, minor, extra)
    middle_total = jnp.sum(received[:, -128])
    final_total = jnp.sum(received[:, -127])
    current = received[:, :-128].reshape(-1)

    current = contract(current, *kernels[2], spread)
    current = contract(current, *kernels[3], spread)

    middle_mean = middle_total / whole_count
    last_mean = final_total / middle_mean / whole_count
    current = current / (middle_mean * last_mean)
    growth = jnp.log(middle_mean) + jnp.log(last_mean)
    return (current, growth)


def solution(mesh):
    in_specs = (P(AXES), P())
    out_specs = (P(AXES), P())
    return jax.shard_map(shards, mesh=mesh, in_specs=in_specs, out_specs=out_specs, check_vma=False)
```

```python
import jax
import jax.numpy as jnp
from jax import lax
from jax.sharding import PartitionSpec as P

BLOCK = 4
WINDOWS = 2
AXES = ("lead", "sub")


def block_kernel(vertical, horizontal, spread):
    position = jnp.arange(spread, dtype=jnp.int32)
    digits = [position // 4 ** (BLOCK - 1 - level) % 4 for level in range(BLOCK)]
    kernel = jnp.ones((spread, spread), jnp.float32)
    for level in range(BLOCK):
        same_spin = (digits[level][:, None] == digits[level][None, :]).astype(jnp.float32)
        kernel = kernel * (1.0 + vertical[level] * same_spin)
    for level in range(1, BLOCK):
        chained = (digits[level - 1] == digits[level]).astype(jnp.float32)
        kernel = kernel * (1.0 + horizontal[level] * chained)[None, :]
    labels = jnp.arange(4, dtype=jnp.int32)
    first_bond = 1.0 + horizontal[0] * (labels[:, None] == labels[None, :]).astype(jnp.float32)
    return (kernel, first_bond)


def multiply(matrix, kernel):
    return lax.dot_general(
        matrix,
        kernel,
        (((0,), (0,)), ((), ())),
        precision=lax.Precision.HIGHEST,
        preferred_element_type=jnp.float32,
    )


def exchange(flat, devices, spread, extra=None):
    shaped = flat.reshape(2, spread, devices, -1)
    rows = jnp.transpose(shaped, (2, 0, 3, 1)).reshape(devices, -1)
    if extra is not None:
        rows = jnp.concatenate([rows, extra], axis=1)
    return lax.all_to_all(rows, AXES, 0, 0, tiled=True)


def contract_middle(flat, kernel, first_bond, spread, low):
    result = lax.dot_general(
        flat.reshape(low, spread, -1),
        kernel,
        (((1,), (0,)), ((), ())),
        precision=lax.Precision.HIGHEST,
        preferred_element_type=jnp.float32,
    )
    bonded = result.reshape(low, -1, 4, 4, spread // 4) * first_bond[None, None, :, :, None]
    return bonded.reshape(-1)


def contract_lead(flat, kernel, first_bond, spread, low):
    result = multiply(flat.reshape(spread, -1), kernel).reshape(low // 4, 4, -1, 4, spread // 4)
    bonded = result * first_bond[None, :, None, :, None]
    return bonded.reshape(-1)


def shards(state, couplings):
    lead_count = lax.axis_size("lead")
    sub_count = lax.axis_size("sub")
    devices = lead_count * sub_count
    me = lax.axis_index("lead") * sub_count + lax.axis_index("sub")
    spread = 4**BLOCK
    whole_count = state.shape[0] * devices
    low = 4**5 // devices
    kernels = []
    for block in range(2 * WINDOWS):
        first_site = block * BLOCK
        kernels.append(
            block_kernel(
                couplings[0, first_site : first_site + BLOCK],
                couplings[1, first_site : first_site + BLOCK],
                spread,
            )
        )

    current = exchange(state, devices, spread).reshape(-1)
    current = contract_lead(current, *kernels[0], spread, low)
    current = contract_middle(current, *kernels[1], spread, low)

    kernel3, bond3 = kernels[2]
    kernel4, bond4 = kernels[3]
    tail = kernel4.reshape(spread, 4, spread // 4).sum(axis=2)
    tail = lax.dot_general(tail, bond4, (((1,), (1,)), ((), ())), precision=lax.Precision.HIGHEST)
    column = jnp.arange(spread, dtype=jnp.int32)
    gather = bond3[:, column // (spread // 4)].T[:, None, :] * tail[:, column % 4].T[:, :, None]
    per_row = spread // devices
    rows = lax.dynamic_slice_in_dim(kernel3, me * per_row, per_row, axis=0)
    weight = lax.dot_general(
        rows, gather.reshape(spread, -1), (((1,), (0,)), ((), ())), precision=lax.Precision.HIGHEST
    ).reshape(per_row, spread, 1, 4)
    middle_part = jnp.sum(current)
    final_part = jnp.sum(current.reshape(per_row, spread, -1, 4) * weight)

    extra = jnp.zeros((devices, 128), jnp.float32)
    extra = extra.at[:, 0].set(middle_part).at[:, 1].set(final_part)
    received = exchange(current, devices, spread, extra)
    middle_total = jnp.sum(received[:, -128])
    final_total = jnp.sum(received[:, -127])
    current = received[:, :-128].reshape(-1)

    current = contract_lead(current, *kernels[2], spread, low)
    current = contract_middle(current, *kernels[3], spread, low)

    middle_mean = middle_total / whole_count
    last_mean = final_total / middle_mean / whole_count
    current = current / (middle_mean * last_mean)
    growth = jnp.log(middle_mean) + jnp.log(last_mean)
    return (current, growth)


def solution(mesh):
    in_specs = (P(AXES), P())
    out_specs = (P(AXES), P())
    return jax.shard_map(shards, mesh=mesh, in_specs=in_specs, out_specs=out_specs, check_vma=False)
```

```python
import jax
import jax.numpy as jnp
from jax import lax
from jax.sharding import PartitionSpec as P

BLOCK = 4
WINDOWS = 2
AXES = ("lead", "sub")
LANES = 128


def block_kernel(vertical, horizontal, spread):
    position = jnp.arange(spread, dtype=jnp.int32)
    digits = [position // 4 ** (BLOCK - 1 - level) % 4 for level in range(BLOCK)]
    kernel = jnp.ones((spread, spread), jnp.float32)
    for level in range(BLOCK):
        same_spin = (digits[level][:, None] == digits[level][None, :]).astype(jnp.float32)
        kernel = kernel * (1.0 + vertical[level] * same_spin)
    for level in range(1, BLOCK):
        chained = (digits[level - 1] == digits[level]).astype(jnp.float32)
        kernel = kernel * (1.0 + horizontal[level] * chained)[None, :]
    labels = jnp.arange(4, dtype=jnp.int32)
    first_bond = 1.0 + horizontal[0] * (labels[:, None] == labels[None, :]).astype(jnp.float32)
    return (kernel, first_bond)


def dot(lhs, rhs, lhs_dims, rhs_dims):
    return lax.dot_general(
        lhs,
        rhs,
        ((lhs_dims, rhs_dims), ((), ())),
        precision=lax.Precision.HIGHEST,
        preferred_element_type=jnp.float32,
    )


def exchange(rows):
    return lax.all_to_all(rows, AXES, 0, 0, tiled=True)


def shards(state, couplings):
    lead_count = lax.axis_size("lead")
    sub_count = lax.axis_size("sub")
    devices = lead_count * sub_count
    me = lax.axis_index("lead") * sub_count + lax.axis_index("sub")
    spread = 4**BLOCK
    quarter = spread // 4
    whole_count = state.shape[0] * devices
    kernels = []
    for block in range(2 * WINDOWS):
        first_site = block * BLOCK
        kernels.append(
            block_kernel(
                couplings[0, first_site : first_site + BLOCK],
                couplings[1, first_site : first_site + BLOCK],
                spread,
            )
        )
    (kernel1, bond1), (kernel2, bond2), (kernel3, bond3), (kernel4, bond4) = kernels
    column = jnp.arange(spread, dtype=jnp.int32)

    received = exchange(state.reshape(-1, LANES).T)
    kernel1 = kernel1 * bond1[me % 4, column // quarter][None, :]
    current = dot(received.reshape(spread, -1), kernel1, (0,), (0,))
    current = dot(current.reshape(spread, -1, spread), kernel2, (0,), (0,))
    pattern2 = bond2[column % 4][:, column // quarter]
    current = current * pattern2[None, :, :]

    tail = kernel4.reshape(spread, 4, quarter).sum(axis=2)
    tail = dot(tail, bond4, (1,), (1,))
    gather = bond3[:, column // quarter].T[:, None, :] * tail[:, column % 4].T[:, :, None]
    per = spread // (devices // 4)
    rows = lax.dynamic_slice_in_dim(kernel3.reshape(per, devices // 4, spread), me // 4, 1, axis=1)
    cols = lax.dynamic_slice_in_dim(gather, (me % 4) * quarter, quarter, axis=1)
    weight = dot(rows.reshape(per, spread), cols.reshape(spread, -1), (1,), (0,))
    weight = weight.reshape(per, quarter, 1, 4)
    selector = (column[:, None] % 4 == jnp.arange(4)[None, :]).astype(jnp.float32)
    marginal = dot(current.reshape(-1, spread), selector, (1,), (0,))
    middle_part = jnp.sum(marginal)
    final_part = jnp.sum(marginal.reshape(per, quarter, 4, 4) * weight)

    sending = current.reshape(per * quarter, -1).T.reshape(devices, -1)
    extra = jnp.zeros((devices, LANES), jnp.float32)
    extra = extra.at[:, 0].set(middle_part).at[:, 1].set(final_part)
    received = exchange(jnp.concatenate([sending, extra], axis=1))
    middle_total = jnp.sum(received[:, -LANES])
    final_total = jnp.sum(received[:, -LANES + 1])
    current = received[:, :-LANES].reshape(devices // 4, 4, 8, per, quarter)
    kernel3 = kernel3.reshape(per, devices // 4, spread).transpose(1, 0, 2)
    current = dot(current, kernel3, (0, 3), (0, 1))
    pattern3 = bond3[jnp.arange(8) % 4][:, column // quarter]
    current = current * pattern3[None, :, None, :]
    current = dot(current, kernel4.reshape(4, quarter, spread), (0, 2), (0, 1))
    pattern4 = bond4[column % 4][:, column // quarter]

    middle_mean = middle_total / whole_count
    last_mean = final_total / middle_mean / whole_count
    current = current * pattern4[None, :, :] / (middle_mean * last_mean)
    growth = jnp.log(middle_mean) + jnp.log(last_mean)
    return (current.reshape(-1), growth)


def solution(mesh):
    in_specs = (P(AXES), P())
    out_specs = (P(AXES), P())
    return jax.shard_map(shards, mesh=mesh, in_specs=in_specs, out_specs=out_specs, check_vma=False)
```

```python
import jax
import jax.numpy as jnp
from jax import lax
from jax.sharding import PartitionSpec as P

BLOCK = 4
WINDOWS = 2
AXES = ("lead", "sub")
LANES = 128


def block_kernel(vertical, horizontal, spread):
    position = jnp.arange(spread, dtype=jnp.int32)
    digits = [position // 4 ** (BLOCK - 1 - level) % 4 for level in range(BLOCK)]
    kernel = jnp.ones((spread, spread), jnp.float32)
    for level in range(BLOCK):
        same_spin = (digits[level][:, None] == digits[level][None, :]).astype(jnp.float32)
        kernel = kernel * (1.0 + vertical[level] * same_spin)
    for level in range(1, BLOCK):
        chained = (digits[level - 1] == digits[level]).astype(jnp.float32)
        kernel = kernel * (1.0 + horizontal[level] * chained)[None, :]
    labels = jnp.arange(4, dtype=jnp.int32)
    first_bond = 1.0 + horizontal[0] * (labels[:, None] == labels[None, :]).astype(jnp.float32)
    return (kernel, first_bond)


def dot(lhs, rhs, lhs_dims, rhs_dims):
    return lax.dot_general(
        lhs,
        rhs,
        ((lhs_dims, rhs_dims), ((), ())),
        precision=lax.Precision.HIGHEST,
        preferred_element_type=jnp.float32,
    )


def exchange(rows):
    devices = rows.shape[0]
    shaped = rows.reshape(devices, -1, LANES)
    return lax.all_to_all(shaped, AXES, 0, 0, tiled=True).reshape(devices, -1)


def shards(state, couplings):
    lead_count = lax.axis_size("lead")
    sub_count = lax.axis_size("sub")
    devices = lead_count * sub_count
    me = lax.axis_index("lead") * sub_count + lax.axis_index("sub")
    spread = 4**BLOCK
    quarter = spread // 4
    whole_count = state.shape[0] * devices
    kernels = []
    for block in range(2 * WINDOWS):
        first_site = block * BLOCK
        kernels.append(
            block_kernel(
                couplings[0, first_site : first_site + BLOCK],
                couplings[1, first_site : first_site + BLOCK],
                spread,
            )
        )
    (kernel1, bond1), (kernel2, bond2), (kernel3, bond3), (kernel4, bond4) = kernels
    column = jnp.arange(spread, dtype=jnp.int32)

    received = exchange(state.reshape(-1, LANES).T)
    kernel1 = kernel1 * bond1[me % 4, column // quarter][None, :]
    current = dot(received.reshape(spread, -1), kernel1, (0,), (0,))
    current = dot(current.reshape(spread, -1, spread), kernel2, (0,), (0,))
    pattern2 = bond2[column % 4][:, column // quarter]
    current = current * pattern2[None, :, :]

    tail = kernel4.reshape(spread, 4, quarter).sum(axis=2)
    tail = dot(tail, bond4, (1,), (1,))
    gather = bond3[:, column // quarter].T[:, None, :] * tail[:, column % 4].T[:, :, None]
    per = spread // (devices // 4)
    rows = lax.dynamic_slice_in_dim(kernel3.reshape(per, devices // 4, spread), me // 4, 1, axis=1)
    cols = lax.dynamic_slice_in_dim(gather, (me % 4) * quarter, quarter, axis=1)
    weight = dot(rows.reshape(per, spread), cols.reshape(spread, -1), (1,), (0,))
    weight = weight.reshape(per, quarter, 1, 4)
    selector = (column[:, None] % 4 == jnp.arange(4)[None, :]).astype(jnp.float32)
    marginal = dot(current.reshape(-1, spread), selector, (1,), (0,))
    middle_part = jnp.sum(marginal)
    final_part = jnp.sum(marginal.reshape(per, quarter, 4, 4) * weight)

    sending = current.reshape(per * quarter, -1).T.reshape(devices, -1)
    extra = jnp.zeros((devices, LANES), jnp.float32)
    extra = extra.at[:, 0].set(middle_part).at[:, 1].set(final_part)
    received = exchange(jnp.concatenate([sending, extra], axis=1))
    middle_total = jnp.sum(received[:, -LANES])
    final_total = jnp.sum(received[:, -LANES + 1])
    current = received[:, :-LANES].reshape(devices // 4, 4, 8, per, quarter)
    kernel3 = kernel3.reshape(per, devices // 4, spread).transpose(1, 0, 2)
    current = dot(current, kernel3, (0, 3), (0, 1))
    pattern3 = bond3[jnp.arange(8) % 4][:, column // quarter]
    current = current * pattern3[None, :, None, :]
    current = dot(current, kernel4.reshape(4, quarter, spread), (0, 2), (0, 1))
    pattern4 = bond4[column % 4][:, column // quarter]

    middle_mean = middle_total / whole_count
    last_mean = final_total / middle_mean / whole_count
    current = current * pattern4[None, :, :] / (middle_mean * last_mean)
    growth = jnp.log(middle_mean) + jnp.log(last_mean)
    return (current.reshape(-1), growth)


def solution(mesh):
    in_specs = (P(AXES), P())
    out_specs = (P(AXES), P())
    return jax.shard_map(shards, mesh=mesh, in_specs=in_specs, out_specs=out_specs, check_vma=False)
```

```python
import jax
import jax.numpy as jnp
from jax import lax
from jax.sharding import PartitionSpec as P

BLOCK = 4
WINDOWS = 2
AXES = ("lead", "sub")
LANES = 128


def block_kernel(vertical, horizontal, spread):
    position = jnp.arange(spread, dtype=jnp.int32)
    digits = [position // 4 ** (BLOCK - 1 - level) % 4 for level in range(BLOCK)]
    kernel = jnp.ones((spread, spread), jnp.float32)
    for level in range(BLOCK):
        same_spin = (digits[level][:, None] == digits[level][None, :]).astype(jnp.float32)
        kernel = kernel * (1.0 + vertical[level] * same_spin)
    for level in range(1, BLOCK):
        chained = (digits[level - 1] == digits[level]).astype(jnp.float32)
        kernel = kernel * (1.0 + horizontal[level] * chained)[None, :]
    labels = jnp.arange(4, dtype=jnp.int32)
    first_bond = 1.0 + horizontal[0] * (labels[:, None] == labels[None, :]).astype(jnp.float32)
    return (kernel, first_bond)


def dot(lhs, rhs, lhs_dims, rhs_dims):
    return lax.dot_general(
        lhs,
        rhs,
        ((lhs_dims, rhs_dims), ((), ())),
        precision=lax.Precision.HIGHEST,
        preferred_element_type=jnp.float32,
    )


def exchange(rows):
    devices = rows.shape[0]
    shaped = rows.reshape(devices, -1, LANES)
    return lax.all_to_all(shaped, AXES, 0, 0, tiled=True).reshape(devices, -1)


def shards(state, couplings):
    lead_count = lax.axis_size("lead")
    sub_count = lax.axis_size("sub")
    devices = lead_count * sub_count
    me = lax.axis_index("lead") * sub_count + lax.axis_index("sub")
    spread = 4**BLOCK
    quarter = spread // 4
    whole_count = state.shape[0] * devices
    kernels = []
    for block in range(2 * WINDOWS):
        first_site = block * BLOCK
        kernels.append(
            block_kernel(
                couplings[0, first_site : first_site + BLOCK],
                couplings[1, first_site : first_site + BLOCK],
                spread,
            )
        )
    (kernel1, bond1), (kernel2, bond2), (kernel3, bond3), (kernel4, bond4) = kernels
    column = jnp.arange(spread, dtype=jnp.int32)

    received = exchange(state.reshape(-1, LANES).T)
    kernel1 = kernel1 * bond1[me % 4, column // quarter][None, :]
    current = dot(received.reshape(spread, -1), kernel1, (0,), (0,))
    current = dot(current.reshape(spread, -1, spread), kernel2, (0,), (0,))
    pattern2 = bond2[column % 4][:, column // quarter]
    current = current * pattern2[None, :, :]

    tail = kernel4.reshape(spread, 4, quarter).sum(axis=2)
    tail = dot(tail, bond4, (1,), (1,))
    gather = bond3[:, column // quarter].T[:, None, :] * tail[:, column % 4].T[:, :, None]
    per = spread // (devices // 4)
    rows = lax.dynamic_slice_in_dim(kernel3.reshape(per, devices // 4, spread), me // 4, 1, axis=1)
    cols = lax.dynamic_slice_in_dim(gather, (me % 4) * quarter, quarter, axis=1)
    weight = dot(rows.reshape(per, spread), cols.reshape(spread, -1), (1,), (0,))
    weight = weight.reshape(per, quarter, 1, 4)
    selector = (column[:, None] % 4 == jnp.arange(4)[None, :]).astype(jnp.float32)
    marginal = dot(current.reshape(-1, spread), selector, (1,), (0,))
    middle_part = jnp.sum(marginal)
    final_part = jnp.sum(marginal.reshape(per, quarter, 4, 4) * weight)

    sending = current.reshape(per * quarter, -1).T.reshape(devices, -1, LANES)
    lane = jnp.arange(LANES, dtype=jnp.int32)
    extra = jnp.where(lane == 0, middle_part, jnp.where(lane == 1, final_part, 0.0))
    extra = jnp.broadcast_to(extra[None, None, :], (devices, 1, LANES))
    received = lax.all_to_all(jnp.concatenate([sending, extra], axis=1), AXES, 0, 0, tiled=True)
    middle_total = jnp.sum(received[:, -1, 0])
    final_total = jnp.sum(received[:, -1, 1])
    received = received[:, :-1, :]
    current = received.reshape(devices // 4, 4, 8, per, quarter)
    kernel3 = kernel3.reshape(per, devices // 4, spread).transpose(1, 0, 2)
    current = dot(current, kernel3, (0, 3), (0, 1))
    pattern3 = bond3[jnp.arange(8) % 4][:, column // quarter]
    current = current * pattern3[None, :, None, :]
    current = dot(current, kernel4.reshape(4, quarter, spread), (0, 2), (0, 1))
    pattern4 = bond4[column % 4][:, column // quarter]

    middle_mean = middle_total / whole_count
    last_mean = final_total / middle_mean / whole_count
    current = current * pattern4[None, :, :] / (middle_mean * last_mean)
    growth = jnp.log(middle_mean) + jnp.log(last_mean)
    return (current.reshape(-1), growth)


def solution(mesh):
    in_specs = (P(AXES), P())
    out_specs = (P(AXES), P())
    return jax.shard_map(shards, mesh=mesh, in_specs=in_specs, out_specs=out_specs, check_vma=False)
```

```python
import jax
import jax.numpy as jnp
from jax import lax
from jax.sharding import PartitionSpec as P

BLOCK = 4
WINDOWS = 2
AXES = ("lead", "sub")
LANES = 128


def block_kernel(vertical, horizontal, spread):
    position = jnp.arange(spread, dtype=jnp.int32)
    digits = [position // 4 ** (BLOCK - 1 - level) % 4 for level in range(BLOCK)]
    kernel = jnp.ones((spread, spread), jnp.float32)
    for level in range(BLOCK):
        same_spin = (digits[level][:, None] == digits[level][None, :]).astype(jnp.float32)
        kernel = kernel * (1.0 + vertical[level] * same_spin)
    for level in range(1, BLOCK):
        chained = (digits[level - 1] == digits[level]).astype(jnp.float32)
        kernel = kernel * (1.0 + horizontal[level] * chained)[None, :]
    labels = jnp.arange(4, dtype=jnp.int32)
    first_bond = 1.0 + horizontal[0] * (labels[:, None] == labels[None, :]).astype(jnp.float32)
    return (kernel, first_bond)


def dot(lhs, rhs, lhs_dims, rhs_dims):
    return lax.dot_general(
        lhs,
        rhs,
        ((lhs_dims, rhs_dims), ((), ())),
        precision=lax.Precision.HIGHEST,
        preferred_element_type=jnp.float32,
    )


def exchange(rows):
    devices = rows.shape[0]
    shaped = rows.reshape(devices, -1, LANES)
    return lax.all_to_all(shaped, AXES, 0, 0, tiled=True).reshape(devices, -1)


def shards(state, couplings):
    lead_count = lax.axis_size("lead")
    sub_count = lax.axis_size("sub")
    devices = lead_count * sub_count
    me = lax.axis_index("lead") * sub_count + lax.axis_index("sub")
    spread = 4**BLOCK
    quarter = spread // 4
    whole_count = state.shape[0] * devices
    kernels = []
    for block in range(2 * WINDOWS):
        first_site = block * BLOCK
        kernels.append(
            block_kernel(
                couplings[0, first_site : first_site + BLOCK],
                couplings[1, first_site : first_site + BLOCK],
                spread,
            )
        )
    (kernel1, bond1), (kernel2, bond2), (kernel3, bond3), (kernel4, bond4) = kernels
    column = jnp.arange(spread, dtype=jnp.int32)

    received = exchange(state.reshape(-1, LANES).T)
    kernel1 = kernel1 * bond1[me % 4, column // quarter][None, :]
    current = dot(received.reshape(spread, -1), kernel1, (0,), (0,))
    current = dot(current.reshape(spread, -1, spread), kernel2, (0,), (0,))
    pattern2 = bond2[column % 4][:, column // quarter]
    current = current * pattern2[None, :, :]

    tail = kernel4.reshape(spread, 4, quarter).sum(axis=2)
    tail = dot(tail, bond4, (1,), (1,))
    gather = bond3[:, column // quarter].T[:, None, :] * tail[:, column % 4].T[:, :, None]
    per = spread // (devices // 4)
    rows = lax.dynamic_slice_in_dim(kernel3.reshape(per, devices // 4, spread), me // 4, 1, axis=1)
    cols = lax.dynamic_slice_in_dim(gather, (me % 4) * quarter, quarter, axis=1)
    weight = dot(rows.reshape(per, spread), cols.reshape(spread, -1), (1,), (0,))
    weight = weight.reshape(per, quarter, 1, 4)
    selector = (column[:, None] % 4 == jnp.arange(4)[None, :]).astype(jnp.float32)
    marginal = dot(current.reshape(-1, spread), selector, (1,), (0,))
    middle_part = jnp.sum(marginal)
    final_part = jnp.sum(marginal.reshape(per, quarter, 4, 4) * weight)

    sending = current.reshape(per * quarter, -1).T.reshape(devices, -1, LANES)
    lane = jnp.arange(LANES, dtype=jnp.int32)
    extra = jnp.where(lane == 0, middle_part, jnp.where(lane == 1, final_part, 0.0))
    extra = jnp.broadcast_to(extra[None, None, :], (devices, 1, LANES))
    half = sending.shape[1] // 2
    first = lax.all_to_all(
        jnp.concatenate([sending[:, :half], extra], axis=1), AXES, 0, 0, tiled=True
    )
    second = lax.all_to_all(sending[:, half:], AXES, 0, 0, tiled=True)
    middle_total = jnp.sum(first[:, -1, 0])
    final_total = jnp.sum(first[:, -1, 1])
    kernel3 = kernel3.reshape(per, devices // 4, spread).transpose(1, 0, 2)
    pattern3 = bond3[jnp.arange(4)][:, column // quarter]
    pattern4 = bond4[column % 4][:, column // quarter]
    kernel4 = kernel4.reshape(4, quarter, spread)
    middle_mean = middle_total / whole_count
    last_mean = final_total / middle_mean / whole_count
    scale = 1.0 / (middle_mean * last_mean)
    outputs = []
    for received in (first[:, :-1], second):
        current = received.reshape(devices // 4, 4, 4, per, quarter)
        current = dot(current, kernel3, (0, 3), (0, 1))
        current = current * pattern3[None, :, None, :]
        current = dot(current, kernel4, (0, 2), (0, 1))
        outputs.append(current * pattern4[None, :, :])
    growth = jnp.log(middle_mean) + jnp.log(last_mean)
    return ((jnp.concatenate(outputs, axis=0) * scale).reshape(-1), growth)


def solution(mesh):
    in_specs = (P(AXES), P())
    out_specs = (P(AXES), P())
    return jax.shard_map(shards, mesh=mesh, in_specs=in_specs, out_specs=out_specs, check_vma=False)
```

```python
import jax
import jax.numpy as jnp
from jax import lax
from jax.sharding import PartitionSpec as P

BLOCK = 4
WINDOWS = 2
AXES = ("lead", "sub")
LANES = 128


def block_kernel(vertical, horizontal, spread):
    position = jnp.arange(spread, dtype=jnp.int32)
    digits = [position // 4 ** (BLOCK - 1 - level) % 4 for level in range(BLOCK)]
    kernel = jnp.ones((spread, spread), jnp.float32)
    for level in range(BLOCK):
        same_spin = (digits[level][:, None] == digits[level][None, :]).astype(jnp.float32)
        kernel = kernel * (1.0 + vertical[level] * same_spin)
    for level in range(1, BLOCK):
        chained = (digits[level - 1] == digits[level]).astype(jnp.float32)
        kernel = kernel * (1.0 + horizontal[level] * chained)[None, :]
    labels = jnp.arange(4, dtype=jnp.int32)
    first_bond = 1.0 + horizontal[0] * (labels[:, None] == labels[None, :]).astype(jnp.float32)
    return (kernel, first_bond)


def dot(lhs, rhs, lhs_dims, rhs_dims, precision=lax.Precision.HIGHEST):
    return lax.dot_general(
        lhs,
        rhs,
        ((lhs_dims, rhs_dims), ((), ())),
        precision=precision,
        preferred_element_type=jnp.float32,
    )


BLOCK_PRECISION = lax.Precision.HIGH


def exchange(rows):
    devices = rows.shape[0]
    shaped = rows.reshape(devices, -1, LANES)
    return lax.all_to_all(shaped, AXES, 0, 0, tiled=True).reshape(devices, -1)


def shards(state, couplings):
    lead_count = lax.axis_size("lead")
    sub_count = lax.axis_size("sub")
    devices = lead_count * sub_count
    me = lax.axis_index("lead") * sub_count + lax.axis_index("sub")
    spread = 4**BLOCK
    quarter = spread // 4
    whole_count = state.shape[0] * devices
    kernels = []
    for block in range(2 * WINDOWS):
        first_site = block * BLOCK
        kernels.append(
            block_kernel(
                couplings[0, first_site : first_site + BLOCK],
                couplings[1, first_site : first_site + BLOCK],
                spread,
            )
        )
    (kernel1, bond1), (kernel2, bond2), (kernel3, bond3), (kernel4, bond4) = kernels
    column = jnp.arange(spread, dtype=jnp.int32)

    received = exchange(state.reshape(-1, LANES).T)
    kernel1 = kernel1 * bond1[me % 4, column // quarter][None, :]
    current = dot(received.reshape(spread, -1), kernel1, (0,), (0,), BLOCK_PRECISION)
    current = dot(current.reshape(spread, -1, spread), kernel2, (0,), (0,), BLOCK_PRECISION)
    pattern2 = bond2[column % 4][:, column // quarter]
    current = current * pattern2[None, :, :]

    tail = kernel4.reshape(spread, 4, quarter).sum(axis=2)
    tail = dot(tail, bond4, (1,), (1,))
    gather = bond3[:, column // quarter].T[:, None, :] * tail[:, column % 4].T[:, :, None]
    per = spread // (devices // 4)
    rows = lax.dynamic_slice_in_dim(kernel3.reshape(per, devices // 4, spread), me // 4, 1, axis=1)
    cols = lax.dynamic_slice_in_dim(gather, (me % 4) * quarter, quarter, axis=1)
    weight = dot(rows.reshape(per, spread), cols.reshape(spread, -1), (1,), (0,))
    weight = weight.reshape(per, quarter, 1, 4)
    selector = (column[:, None] % 4 == jnp.arange(4)[None, :]).astype(jnp.float32)
    marginal = dot(current.reshape(-1, spread), selector, (1,), (0,))
    middle_part = jnp.sum(marginal)
    final_part = jnp.sum(marginal.reshape(per, quarter, 4, 4) * weight)

    sending = current.reshape(per * quarter, -1).T.reshape(devices, -1, LANES)
    lane = jnp.arange(LANES, dtype=jnp.int32)
    extra = jnp.where(lane == 0, middle_part, jnp.where(lane == 1, final_part, 0.0))
    extra = jnp.broadcast_to(extra[None, None, :], (devices, 1, LANES))
    received = lax.all_to_all(jnp.concatenate([sending, extra], axis=1), AXES, 0, 0, tiled=True)
    middle_total = jnp.sum(received[:, -1, 0])
    final_total = jnp.sum(received[:, -1, 1])
    received = received[:, :-1, :]
    current = received.reshape(devices // 4, 4, 8, per, quarter)
    kernel3 = kernel3.reshape(per, devices // 4, spread).transpose(1, 0, 2)
    current = dot(current, kernel3, (0, 3), (0, 1), BLOCK_PRECISION)
    pattern3 = bond3[jnp.arange(8) % 4][:, column // quarter]
    current = current * pattern3[None, :, None, :]
    current = dot(current, kernel4.reshape(4, quarter, spread), (0, 2), (0, 1), BLOCK_PRECISION)
    pattern4 = bond4[column % 4][:, column // quarter]

    middle_mean = middle_total / whole_count
    last_mean = final_total / middle_mean / whole_count
    current = current * pattern4[None, :, :] / (middle_mean * last_mean)
    growth = jnp.log(middle_mean) + jnp.log(last_mean)
    return (current.reshape(-1), growth)


def solution(mesh):
    in_specs = (P(AXES), P())
    out_specs = (P(AXES), P())
    return jax.shard_map(shards, mesh=mesh, in_specs=in_specs, out_specs=out_specs, check_vma=False)
```

```python
import jax
import jax.numpy as jnp
from jax import lax
from jax.sharding import PartitionSpec as P

BLOCK = 4
WINDOWS = 2
AXES = ("lead", "sub")
LANES = 128


def block_kernel(vertical, horizontal, spread):
    position = jnp.arange(spread, dtype=jnp.int32)
    digits = [position // 4 ** (BLOCK - 1 - level) % 4 for level in range(BLOCK)]
    kernel = jnp.ones((spread, spread), jnp.float32)
    for level in range(BLOCK):
        same_spin = (digits[level][:, None] == digits[level][None, :]).astype(jnp.float32)
        kernel = kernel * (1.0 + vertical[level] * same_spin)
    for level in range(1, BLOCK):
        chained = (digits[level - 1] == digits[level]).astype(jnp.float32)
        kernel = kernel * (1.0 + horizontal[level] * chained)[None, :]
    labels = jnp.arange(4, dtype=jnp.int32)
    first_bond = 1.0 + horizontal[0] * (labels[:, None] == labels[None, :]).astype(jnp.float32)
    return (kernel, first_bond)


def dot(lhs, rhs, lhs_dims, rhs_dims, precision=lax.Precision.HIGHEST):
    return lax.dot_general(
        lhs,
        rhs,
        ((lhs_dims, rhs_dims), ((), ())),
        precision=precision,
        preferred_element_type=jnp.float32,
    )


BLOCK_PRECISION = lax.Precision.HIGH


def exchange(rows):
    devices = rows.shape[0]
    shaped = rows.reshape(devices, -1, LANES)
    return lax.all_to_all(shaped, AXES, 0, 0, tiled=True).reshape(devices, -1)


def shards(state, couplings):
    lead_count = lax.axis_size("lead")
    sub_count = lax.axis_size("sub")
    devices = lead_count * sub_count
    me = lax.axis_index("lead") * sub_count + lax.axis_index("sub")
    spread = 4**BLOCK
    quarter = spread // 4
    whole_count = state.shape[0] * devices
    kernels = []
    for block in range(2 * WINDOWS):
        first_site = block * BLOCK
        kernels.append(
            block_kernel(
                couplings[0, first_site : first_site + BLOCK],
                couplings[1, first_site : first_site + BLOCK],
                spread,
            )
        )
    (kernel1, bond1), (kernel2, bond2), (kernel3, bond3), (kernel4, bond4) = kernels
    column = jnp.arange(spread, dtype=jnp.int32)

    sending = jnp.transpose(state.reshape(2, spread, -1, LANES), (3, 0, 2, 1))
    received = exchange(sending.reshape(devices, -1))
    kernel1 = kernel1 * bond1[me % 4, column // quarter][None, :]
    current = dot(kernel1, received.reshape(spread, -1), (0,), (0,), BLOCK_PRECISION)
    current = dot(current.reshape(-1, spread), kernel2, (1,), (0,), BLOCK_PRECISION)
    pattern2 = bond2[column % 4][:, column // quarter]
    current = current.reshape(spread, -1, spread) * pattern2[:, None, :]
    current = jnp.transpose(current, (1, 0, 2))

    tail = kernel4.reshape(spread, 4, quarter).sum(axis=2)
    tail = dot(tail, bond4, (1,), (1,))
    gather = bond3[:, column // quarter].T[:, None, :] * tail[:, column % 4].T[:, :, None]
    per = spread // (devices // 4)
    rows = lax.dynamic_slice_in_dim(kernel3.reshape(per, devices // 4, spread), me // 4, 1, axis=1)
    cols = lax.dynamic_slice_in_dim(gather, (me % 4) * quarter, quarter, axis=1)
    weight = dot(rows.reshape(per, spread), cols.reshape(spread, -1), (1,), (0,))
    weight = weight.reshape(per, quarter, 1, 4)
    selector = (column[:, None] % 4 == jnp.arange(4)[None, :]).astype(jnp.float32)
    marginal = dot(current.reshape(-1, spread), selector, (1,), (0,))
    middle_part = jnp.sum(marginal)
    final_part = jnp.sum(marginal.reshape(per, quarter, 4, 4) * weight)

    sending = current.reshape(per * quarter, -1).T.reshape(devices, -1, LANES)
    lane = jnp.arange(LANES, dtype=jnp.int32)
    extra = jnp.where(lane == 0, middle_part, jnp.where(lane == 1, final_part, 0.0))
    extra = jnp.broadcast_to(extra[None, None, :], (devices, 1, LANES))
    received = lax.all_to_all(jnp.concatenate([sending, extra], axis=1), AXES, 0, 0, tiled=True)
    middle_total = jnp.sum(received[:, -1, 0])
    final_total = jnp.sum(received[:, -1, 1])
    received = received[:, :-1, :]
    current = received.reshape(devices // 4, 4, 8, per, quarter)
    kernel3 = kernel3.reshape(per, devices // 4, spread).transpose(1, 0, 2)
    current = dot(current, kernel3, (0, 3), (0, 1), BLOCK_PRECISION)
    pattern3 = bond3[jnp.arange(8) % 4][:, column // quarter]
    current = current * pattern3[None, :, None, :]
    current = dot(current, kernel4.reshape(4, quarter, spread), (0, 2), (0, 1), BLOCK_PRECISION)
    pattern4 = bond4[column % 4][:, column // quarter]

    middle_mean = middle_total / whole_count
    last_mean = final_total / middle_mean / whole_count
    current = current * pattern4[None, :, :] / (middle_mean * last_mean)
    growth = jnp.log(middle_mean) + jnp.log(last_mean)
    return (current.reshape(-1), growth)


def solution(mesh):
    in_specs = (P(AXES), P())
    out_specs = (P(AXES), P())
    return jax.shard_map(shards, mesh=mesh, in_specs=in_specs, out_specs=out_specs, check_vma=False)
```

```python
import jax
import jax.numpy as jnp
from jax import lax
from jax.sharding import PartitionSpec as P

BLOCK = 4
WINDOWS = 2
AXES = ("lead", "sub")
LANES = 128


def block_kernel(vertical, horizontal, spread):
    position = jnp.arange(spread, dtype=jnp.int32)
    digits = [position // 4 ** (BLOCK - 1 - level) % 4 for level in range(BLOCK)]
    kernel = jnp.ones((spread, spread), jnp.float32)
    for level in range(BLOCK):
        same_spin = (digits[level][:, None] == digits[level][None, :]).astype(jnp.float32)
        kernel = kernel * (1.0 + vertical[level] * same_spin)
    for level in range(1, BLOCK):
        chained = (digits[level - 1] == digits[level]).astype(jnp.float32)
        kernel = kernel * (1.0 + horizontal[level] * chained)[None, :]
    labels = jnp.arange(4, dtype=jnp.int32)
    first_bond = 1.0 + horizontal[0] * (labels[:, None] == labels[None, :]).astype(jnp.float32)
    return (kernel, first_bond)


def dot(lhs, rhs, lhs_dims, rhs_dims, precision=lax.Precision.HIGHEST):
    return lax.dot_general(
        lhs,
        rhs,
        ((lhs_dims, rhs_dims), ((), ())),
        precision=precision,
        preferred_element_type=jnp.float32,
    )


BLOCK_PRECISION = lax.Precision.HIGH


def exchange(rows):
    devices = rows.shape[0]
    shaped = rows.reshape(devices, -1, LANES)
    return lax.all_to_all(shaped, AXES, 0, 0, tiled=True).reshape(devices, -1)


def shards(state, couplings):
    lead_count = lax.axis_size("lead")
    sub_count = lax.axis_size("sub")
    devices = lead_count * sub_count
    me = lax.axis_index("lead") * sub_count + lax.axis_index("sub")
    spread = 4**BLOCK
    quarter = spread // 4
    whole_count = state.shape[0] * devices
    kernels = []
    for block in range(2 * WINDOWS):
        first_site = block * BLOCK
        kernels.append(
            block_kernel(
                couplings[0, first_site : first_site + BLOCK],
                couplings[1, first_site : first_site + BLOCK],
                spread,
            )
        )
    (kernel1, bond1), (kernel2, bond2), (kernel3, bond3), (kernel4, bond4) = kernels
    column = jnp.arange(spread, dtype=jnp.int32)

    sending = jnp.transpose(state.reshape(2, spread, -1, LANES), (3, 0, 2, 1))
    received = lax.all_to_all(sending, AXES, 0, 0, tiled=True)
    kernel1 = kernel1 * bond1[me % 4, column // quarter][None, :]
    current = dot(kernel1, received.reshape(spread, -1, spread), (0,), (0,), BLOCK_PRECISION)
    current = dot(current.reshape(-1, spread), kernel2, (1,), (0,), BLOCK_PRECISION)
    pattern2 = bond2[column % 4][:, column // quarter]
    current = current.reshape(spread, -1, spread) * pattern2[:, None, :]
    current = jnp.transpose(current, (1, 0, 2))

    tail = kernel4.reshape(spread, 4, quarter).sum(axis=2)
    tail = dot(tail, bond4, (1,), (1,))
    gather = bond3[:, column // quarter].T[:, None, :] * tail[:, column % 4].T[:, :, None]
    per = spread // (devices // 4)
    rows = lax.dynamic_slice_in_dim(kernel3.reshape(per, devices // 4, spread), me // 4, 1, axis=1)
    cols = lax.dynamic_slice_in_dim(gather, (me % 4) * quarter, quarter, axis=1)
    weight = dot(rows.reshape(per, spread), cols.reshape(spread, -1), (1,), (0,))
    weight = weight.reshape(per, quarter, 1, 4)
    selector = (column[:, None] % 4 == jnp.arange(4)[None, :]).astype(jnp.float32)
    marginal = dot(current.reshape(-1, spread), selector, (1,), (0,))
    middle_part = jnp.sum(marginal)
    final_part = jnp.sum(marginal.reshape(per, quarter, 4, 4) * weight)

    sending = current.reshape(per * quarter, -1).T.reshape(devices, -1, LANES)
    lane = jnp.arange(LANES, dtype=jnp.int32)
    extra = jnp.where(lane == 0, middle_part, jnp.where(lane == 1, final_part, 0.0))
    extra = jnp.broadcast_to(extra[None, None, :], (devices, 1, LANES))
    received = lax.all_to_all(jnp.concatenate([sending, extra], axis=1), AXES, 0, 0, tiled=True)
    middle_total = jnp.sum(received[:, -1, 0])
    final_total = jnp.sum(received[:, -1, 1])
    received = received[:, :-1, :]
    current = received.reshape(devices // 4, 4, 8, per, quarter)
    kernel3 = kernel3.reshape(per, devices // 4, spread).transpose(1, 0, 2)
    current = dot(current, kernel3, (0, 3), (0, 1), BLOCK_PRECISION)
    pattern3 = bond3[jnp.arange(8) % 4][:, column // quarter]
    current = current * pattern3[None, :, None, :]
    current = dot(current, kernel4.reshape(4, quarter, spread), (0, 2), (0, 1), BLOCK_PRECISION)
    pattern4 = bond4[column % 4][:, column // quarter]

    middle_mean = middle_total / whole_count
    last_mean = final_total / middle_mean / whole_count
    current = current * pattern4[None, :, :] / (middle_mean * last_mean)
    growth = jnp.log(middle_mean) + jnp.log(last_mean)
    return (current.reshape(-1), growth)


def solution(mesh):
    in_specs = (P(AXES), P())
    out_specs = (P(AXES), P())
    return jax.shard_map(shards, mesh=mesh, in_specs=in_specs, out_specs=out_specs, check_vma=False)
```

```python
import jax
import jax.numpy as jnp
from jax import lax
from jax.sharding import PartitionSpec as P

BLOCK = 4
WINDOWS = 2
AXES = ("lead", "sub")
LANES = 128


def block_kernel(vertical, horizontal, spread):
    position = jnp.arange(spread, dtype=jnp.int32)
    digits = [position // 4 ** (BLOCK - 1 - level) % 4 for level in range(BLOCK)]
    kernel = jnp.ones((spread, spread), jnp.float32)
    for level in range(BLOCK):
        same_spin = (digits[level][:, None] == digits[level][None, :]).astype(jnp.float32)
        kernel = kernel * (1.0 + vertical[level] * same_spin)
    for level in range(1, BLOCK):
        chained = (digits[level - 1] == digits[level]).astype(jnp.float32)
        kernel = kernel * (1.0 + horizontal[level] * chained)[None, :]
    labels = jnp.arange(4, dtype=jnp.int32)
    first_bond = 1.0 + horizontal[0] * (labels[:, None] == labels[None, :]).astype(jnp.float32)
    return (kernel, first_bond)


def dot(lhs, rhs, lhs_dims, rhs_dims, precision=lax.Precision.HIGHEST):
    return lax.dot_general(
        lhs,
        rhs,
        ((lhs_dims, rhs_dims), ((), ())),
        precision=precision,
        preferred_element_type=jnp.float32,
    )


BLOCK_PRECISION = lax.Precision.HIGH


def exchange(rows):
    devices = rows.shape[0]
    shaped = rows.reshape(devices, -1, LANES)
    return lax.all_to_all(shaped, AXES, 0, 0, tiled=True).reshape(devices, -1)


def shards(state, couplings):
    lead_count = lax.axis_size("lead")
    sub_count = lax.axis_size("sub")
    devices = lead_count * sub_count
    me = lax.axis_index("lead") * sub_count + lax.axis_index("sub")
    spread = 4**BLOCK
    quarter = spread // 4
    whole_count = state.shape[0] * devices
    kernels = []
    for block in range(2 * WINDOWS):
        first_site = block * BLOCK
        kernels.append(
            block_kernel(
                couplings[0, first_site : first_site + BLOCK],
                couplings[1, first_site : first_site + BLOCK],
                spread,
            )
        )
    (kernel1, bond1), (kernel2, bond2), (kernel3, bond3), (kernel4, bond4) = kernels
    column = jnp.arange(spread, dtype=jnp.int32)

    sending = jnp.transpose(state.reshape(2, spread, -1, LANES), (3, 0, 2, 1))
    received = lax.all_to_all(sending, AXES, 0, 0, tiled=True)
    kernel1 = kernel1 * bond1[me % 4, column // quarter][None, :]
    kernel1 = kernel1.reshape(spread, quarter, 4).transpose(0, 2, 1).reshape(spread, spread)
    current = dot(kernel1, received.reshape(spread, -1, spread), (0,), (0,), BLOCK_PRECISION)
    current = dot(current.reshape(-1, spread), kernel2, (1,), (0,), BLOCK_PRECISION)
    pattern2 = bond2[column // quarter][:, column // quarter]
    current = current.reshape(spread, -1, spread) * pattern2[:, None, :]
    current = jnp.transpose(current, (1, 0, 2))

    tail = kernel4.reshape(spread, 4, quarter).sum(axis=2)
    tail = dot(tail, bond4, (1,), (1,))
    gather = bond3[:, column // quarter].T[:, None, :] * tail[:, column % 4].T[:, :, None]
    per = spread // (devices // 4)
    rows = lax.dynamic_slice_in_dim(kernel3.reshape(per, devices // 4, spread), me // 4, 1, axis=1)
    cols = lax.dynamic_slice_in_dim(gather, (me % 4) * quarter, quarter, axis=1)
    weight = dot(rows.reshape(per, spread), cols.reshape(spread, -1), (1,), (0,))
    weight = weight.reshape(per, 1, quarter, 4)
    selector = (column[:, None] % 4 == jnp.arange(4)[None, :]).astype(jnp.float32)
    marginal = dot(current.reshape(-1, spread), selector, (1,), (0,))
    middle_part = jnp.sum(marginal)
    final_part = jnp.sum(marginal.reshape(per, 4, quarter, 4) * weight)

    sending = jnp.transpose(current.reshape(per, 4, quarter, spread), (1, 3, 0, 2))
    sending = sending.reshape(devices, -1, LANES)
    lane = jnp.arange(LANES, dtype=jnp.int32)
    extra = jnp.where(lane == 0, middle_part, jnp.where(lane == 1, final_part, 0.0))
    extra = jnp.broadcast_to(extra[None, None, :], (devices, 1, LANES))
    received = lax.all_to_all(jnp.concatenate([sending, extra], axis=1), AXES, 0, 0, tiled=True)
    middle_total = jnp.sum(received[:, -1, 0])
    final_total = jnp.sum(received[:, -1, 1])
    received = received[:, :-1, :]
    current = received.reshape(devices // 4, 4, 8, per, quarter)
    kernel3 = kernel3.reshape(per, devices // 4, spread).transpose(1, 0, 2)
    current = dot(current, kernel3, (0, 3), (0, 1), BLOCK_PRECISION)
    pattern3 = bond3[jnp.arange(8) % 4][:, column // quarter]
    current = current * pattern3[None, :, None, :]
    current = dot(current, kernel4.reshape(4, quarter, spread), (0, 2), (0, 1), BLOCK_PRECISION)
    pattern4 = bond4[column % 4][:, column // quarter]

    middle_mean = middle_total / whole_count
    last_mean = final_total / middle_mean / whole_count
    current = current * pattern4[None, :, :] / (middle_mean * last_mean)
    growth = jnp.log(middle_mean) + jnp.log(last_mean)
    return (current.reshape(-1), growth)


def solution(mesh):
    in_specs = (P(AXES), P())
    out_specs = (P(AXES), P())
    return jax.shard_map(shards, mesh=mesh, in_specs=in_specs, out_specs=out_specs, check_vma=False)
```

```python
import jax
import jax.numpy as jnp
from jax import lax
from jax.sharding import PartitionSpec as P

BLOCK = 4
WINDOWS = 2
AXES = ("lead", "sub")
LANES = 128


def block_kernel(vertical, horizontal, spread):
    position = jnp.arange(spread, dtype=jnp.int32)
    digits = [position // 4 ** (BLOCK - 1 - level) % 4 for level in range(BLOCK)]
    kernel = jnp.ones((spread, spread), jnp.float32)
    for level in range(BLOCK):
        same_spin = (digits[level][:, None] == digits[level][None, :]).astype(jnp.float32)
        kernel = kernel * (1.0 + vertical[level] * same_spin)
    for level in range(1, BLOCK):
        chained = (digits[level - 1] == digits[level]).astype(jnp.float32)
        kernel = kernel * (1.0 + horizontal[level] * chained)[None, :]
    labels = jnp.arange(4, dtype=jnp.int32)
    first_bond = 1.0 + horizontal[0] * (labels[:, None] == labels[None, :]).astype(jnp.float32)
    return (kernel, first_bond)


def dot(lhs, rhs, lhs_dims, rhs_dims, precision=lax.Precision.HIGHEST):
    return lax.dot_general(
        lhs,
        rhs,
        ((lhs_dims, rhs_dims), ((), ())),
        precision=precision,
        preferred_element_type=jnp.float32,
    )


BLOCK_PRECISION = lax.Precision.HIGH


def exchange(rows):
    devices = rows.shape[0]
    shaped = rows.reshape(devices, -1, LANES)
    return lax.all_to_all(shaped, AXES, 0, 0, tiled=True).reshape(devices, -1)


def shards(state, couplings):
    lead_count = lax.axis_size("lead")
    sub_count = lax.axis_size("sub")
    devices = lead_count * sub_count
    me = lax.axis_index("lead") * sub_count + lax.axis_index("sub")
    spread = 4**BLOCK
    quarter = spread // 4
    whole_count = state.shape[0] * devices
    kernels = []
    for block in range(2 * WINDOWS):
        first_site = block * BLOCK
        kernels.append(
            block_kernel(
                couplings[0, first_site : first_site + BLOCK],
                couplings[1, first_site : first_site + BLOCK],
                spread,
            )
        )
    (kernel1, bond1), (kernel2, bond2), (kernel3, bond3), (kernel4, bond4) = kernels
    column = jnp.arange(spread, dtype=jnp.int32)

    sending = jnp.transpose(state.reshape(2, spread, -1, LANES), (3, 0, 2, 1))
    received = lax.all_to_all(sending, AXES, 0, 0, tiled=True)
    kernel1 = kernel1 * bond1[me % 4, column // quarter][None, :]
    current = dot(kernel1, received.reshape(spread, -1, spread), (0,), (0,), BLOCK_PRECISION)
    current = dot(current.reshape(-1, spread), kernel2, (1,), (0,), BLOCK_PRECISION)
    pattern2 = bond2[column % 4][:, column // quarter]
    current = current.reshape(spread, -1, spread) * pattern2[:, None, :]
    current = jnp.transpose(current, (1, 0, 2))

    tail = kernel4.reshape(spread, 4, quarter).sum(axis=2)
    tail = dot(tail, bond4, (1,), (1,))
    gather = bond3[:, column // quarter].T[:, None, :] * tail[:, column % 4].T[:, :, None]
    per = spread // (devices // 4)
    rows = lax.dynamic_slice_in_dim(kernel3.reshape(per, devices // 4, spread), me // 4, 1, axis=1)
    cols = lax.dynamic_slice_in_dim(gather, (me % 4) * quarter, quarter, axis=1)
    weight = dot(rows.reshape(per, spread), cols.reshape(spread, -1), (1,), (0,))
    weight = weight.reshape(per, quarter, 1, 4)
    selector = (column[:, None] % 4 == jnp.arange(4)[None, :]).astype(jnp.float32)
    marginal = dot(current.reshape(-1, spread), selector, (1,), (0,))
    middle_part = jnp.sum(marginal)
    final_part = jnp.sum(marginal.reshape(per, quarter, 4, 4) * weight)

    sending = current.reshape(per * quarter, -1).T.reshape(devices, -1, LANES)
    lane = jnp.arange(LANES, dtype=jnp.int32)
    extra = jnp.where(lane == 0, middle_part, jnp.where(lane == 1, final_part, 0.0))
    extra = jnp.broadcast_to(extra[None, None, :], (devices, 1, LANES))
    payload = jnp.concatenate([sending, extra], axis=1)
    lead_part = payload.reshape(lead_count, sub_count, -1, LANES)
    lead_part = lax.all_to_all(lead_part, "sub", 1, 1, tiled=True)
    received = lax.all_to_all(lead_part, "lead", 0, 0, tiled=True).reshape(devices, -1, LANES)
    middle_total = jnp.sum(received[:, -1, 0])
    final_total = jnp.sum(received[:, -1, 1])
    received = received[:, :-1, :]
    current = received.reshape(devices // 4, 4, 8, per, quarter)
    kernel3 = kernel3.reshape(per, devices // 4, spread).transpose(1, 0, 2)
    current = dot(current, kernel3, (0, 3), (0, 1), BLOCK_PRECISION)
    pattern3 = bond3[jnp.arange(8) % 4][:, column // quarter]
    current = current * pattern3[None, :, None, :]
    current = dot(current, kernel4.reshape(4, quarter, spread), (0, 2), (0, 1), BLOCK_PRECISION)
    pattern4 = bond4[column % 4][:, column // quarter]

    middle_mean = middle_total / whole_count
    last_mean = final_total / middle_mean / whole_count
    current = current * pattern4[None, :, :] / (middle_mean * last_mean)
    growth = jnp.log(middle_mean) + jnp.log(last_mean)
    return (current.reshape(-1), growth)


def solution(mesh):
    in_specs = (P(AXES), P())
    out_specs = (P(AXES), P())
    return jax.shard_map(shards, mesh=mesh, in_specs=in_specs, out_specs=out_specs, check_vma=False)
```

```python
import jax
import jax.numpy as jnp
from jax import lax
from jax.sharding import PartitionSpec as P

BLOCK = 4
WINDOWS = 2
AXES = ("lead", "sub")
LANES = 128


def block_kernel(vertical, horizontal, spread):
    position = jnp.arange(spread, dtype=jnp.int32)
    digits = [position // 4 ** (BLOCK - 1 - level) % 4 for level in range(BLOCK)]
    kernel = jnp.ones((spread, spread), jnp.float32)
    for level in range(BLOCK):
        same_spin = (digits[level][:, None] == digits[level][None, :]).astype(jnp.float32)
        kernel = kernel * (1.0 + vertical[level] * same_spin)
    for level in range(1, BLOCK):
        chained = (digits[level - 1] == digits[level]).astype(jnp.float32)
        kernel = kernel * (1.0 + horizontal[level] * chained)[None, :]
    labels = jnp.arange(4, dtype=jnp.int32)
    first_bond = 1.0 + horizontal[0] * (labels[:, None] == labels[None, :]).astype(jnp.float32)
    return (kernel, first_bond)


def dot(lhs, rhs, lhs_dims, rhs_dims, precision=lax.Precision.HIGHEST):
    return lax.dot_general(
        lhs,
        rhs,
        ((lhs_dims, rhs_dims), ((), ())),
        precision=precision,
        preferred_element_type=jnp.float32,
    )


BLOCK_PRECISION = lax.Precision.HIGH


def exchange(rows):
    devices = rows.shape[0]
    shaped = rows.reshape(devices, -1, LANES)
    return lax.all_to_all(shaped, AXES, 0, 0, tiled=True).reshape(devices, -1)


def shards(state, couplings):
    lead_count = lax.axis_size("lead")
    sub_count = lax.axis_size("sub")
    devices = lead_count * sub_count
    me = lax.axis_index("lead") * sub_count + lax.axis_index("sub")
    spread = 4**BLOCK
    quarter = spread // 4
    whole_count = state.shape[0] * devices
    kernels = []
    for block in range(2 * WINDOWS):
        first_site = block * BLOCK
        kernels.append(
            block_kernel(
                couplings[0, first_site : first_site + BLOCK],
                couplings[1, first_site : first_site + BLOCK],
                spread,
            )
        )
    (kernel1, bond1), (kernel2, bond2), (kernel3, bond3), (kernel4, bond4) = kernels
    column = jnp.arange(spread, dtype=jnp.int32)

    sending = jnp.transpose(state.reshape(2, spread, -1, LANES), (3, 0, 2, 1))
    received = lax.all_to_all(sending, AXES, 0, 0, tiled=True)
    kernel1 = kernel1 * bond1[me % 4, column // quarter][None, :]
    current = dot(kernel1, received.reshape(spread, -1, spread), (0,), (0,), BLOCK_PRECISION)
    current = dot(current.reshape(-1, spread), kernel2, (1,), (0,), BLOCK_PRECISION)
    pattern2 = bond2[column % 4][:, column // quarter]
    current = current.reshape(spread, -1, spread) * pattern2[:, None, :]
    current = jnp.transpose(current, (1, 0, 2))

    tail = kernel4.reshape(spread, 4, quarter).sum(axis=2)
    tail = dot(tail, bond4, (1,), (1,))
    gather = bond3[:, column // quarter].T[:, None, :] * tail[:, column % 4].T[:, :, None]
    per = spread // (devices // 4)
    rows = lax.dynamic_slice_in_dim(kernel3.reshape(per, devices // 4, spread), me // 4, 1, axis=1)
    cols = lax.dynamic_slice_in_dim(gather, (me % 4) * quarter, quarter, axis=1)
    weight = dot(rows.reshape(per, spread), cols.reshape(spread, -1), (1,), (0,))
    weight = weight.reshape(per, quarter, 1, 4)
    selector = (column[:, None] % 4 == jnp.arange(4)[None, :]).astype(jnp.float32)
    marginal = dot(current.reshape(-1, spread), selector, (1,), (0,))
    middle_part = jnp.sum(marginal)
    final_part = jnp.sum(marginal.reshape(per, quarter, 4, 4) * weight)

    sending = current.reshape(per * quarter, -1).T.reshape(devices, -1, LANES)
    middle_row = jnp.broadcast_to(middle_part, (devices, 1, LANES))
    final_row = jnp.broadcast_to(final_part, (devices, 1, LANES))
    payload = jnp.concatenate([sending, middle_row, final_row], axis=1)
    received = lax.all_to_all(payload, AXES, 0, 0, tiled=True)
    middle_total = jnp.sum(received[:, -2, 0])
    final_total = jnp.sum(received[:, -1, 0])
    received = received[:, :-2, :]
    current = received.reshape(devices // 4, 4, 8, per, quarter)
    kernel3 = kernel3.reshape(per, devices // 4, spread).transpose(1, 0, 2)
    current = dot(current, kernel3, (0, 3), (0, 1), BLOCK_PRECISION)
    pattern3 = bond3[jnp.arange(8) % 4][:, column // quarter]
    current = current * pattern3[None, :, None, :]
    current = dot(current, kernel4.reshape(4, quarter, spread), (0, 2), (0, 1), BLOCK_PRECISION)
    pattern4 = bond4[column % 4][:, column // quarter]

    middle_mean = middle_total / whole_count
    last_mean = final_total / middle_mean / whole_count
    current = current * pattern4[None, :, :] / (middle_mean * last_mean)
    growth = jnp.log(middle_mean) + jnp.log(last_mean)
    return (current.reshape(-1), growth)


def solution(mesh):
    in_specs = (P(AXES), P())
    out_specs = (P(AXES), P())
    return jax.shard_map(shards, mesh=mesh, in_specs=in_specs, out_specs=out_specs, check_vma=False)
```

```python
import jax
import jax.numpy as jnp
from jax import lax
from jax.sharding import PartitionSpec as P

BLOCK = 4
WINDOWS = 2
AXES = ("lead", "sub")
LANES = 128


def block_kernel(vertical, horizontal, spread):
    position = jnp.arange(spread, dtype=jnp.int32)
    digits = [position // 4 ** (BLOCK - 1 - level) % 4 for level in range(BLOCK)]
    kernel = jnp.ones((spread, spread), jnp.float32)
    for level in range(BLOCK):
        same_spin = (digits[level][:, None] == digits[level][None, :]).astype(jnp.float32)
        kernel = kernel * (1.0 + vertical[level] * same_spin)
    for level in range(1, BLOCK):
        chained = (digits[level - 1] == digits[level]).astype(jnp.float32)
        kernel = kernel * (1.0 + horizontal[level] * chained)[None, :]
    labels = jnp.arange(4, dtype=jnp.int32)
    first_bond = 1.0 + horizontal[0] * (labels[:, None] == labels[None, :]).astype(jnp.float32)
    return (kernel, first_bond)


def dot(lhs, rhs, lhs_dims, rhs_dims, precision=lax.Precision.HIGHEST):
    return lax.dot_general(
        lhs,
        rhs,
        ((lhs_dims, rhs_dims), ((), ())),
        precision=precision,
        preferred_element_type=jnp.float32,
    )


BLOCK_PRECISION = lax.Precision.HIGH


def exchange(rows):
    devices = rows.shape[0]
    shaped = rows.reshape(devices, -1, LANES)
    return lax.all_to_all(shaped, AXES, 0, 0, tiled=True).reshape(devices, -1)


def shards(state, couplings):
    lead_count = lax.axis_size("lead")
    sub_count = lax.axis_size("sub")
    devices = lead_count * sub_count
    me = lax.axis_index("lead") * sub_count + lax.axis_index("sub")
    spread = 4**BLOCK
    quarter = spread // 4
    whole_count = state.shape[0] * devices
    kernels = []
    for block in range(2 * WINDOWS):
        first_site = block * BLOCK
        kernels.append(
            block_kernel(
                couplings[0, first_site : first_site + BLOCK],
                couplings[1, first_site : first_site + BLOCK],
                spread,
            )
        )
    (kernel1, bond1), (kernel2, bond2), (kernel3, bond3), (kernel4, bond4) = kernels
    column = jnp.arange(spread, dtype=jnp.int32)

    sending = jnp.transpose(state.reshape(2, spread, -1, LANES), (3, 0, 2, 1))
    received = lax.all_to_all(sending, AXES, 0, 0, tiled=True)
    kernel1 = kernel1 * bond1[me % 4, column // quarter][None, :]
    current = dot(kernel1, received.reshape(spread, -1, spread), (0,), (0,), BLOCK_PRECISION)
    current = dot(current.reshape(-1, spread), kernel2, (1,), (0,), BLOCK_PRECISION)
    pattern2 = bond2[column % 4][:, column // quarter]
    current = current.reshape(spread, -1, spread) * pattern2[:, None, :]
    current = jnp.transpose(current, (1, 0, 2))

    tail = kernel4.reshape(spread, 4, quarter).sum(axis=2)
    tail = dot(tail, bond4, (1,), (1,))
    gather = bond3[:, column // quarter].T[:, None, :] * tail[:, column % 4].T[:, :, None]
    per = spread // (devices // 4)
    rows = lax.dynamic_slice_in_dim(kernel3.reshape(per, devices // 4, spread), me // 4, 1, axis=1)
    cols = lax.dynamic_slice_in_dim(gather, (me % 4) * quarter, quarter, axis=1)
    weight = dot(rows.reshape(per, spread), cols.reshape(spread, -1), (1,), (0,))
    weight = weight.reshape(per, quarter, 1, 4)
    selector = (column[:, None] % 4 == jnp.arange(4)[None, :]).astype(jnp.float32)
    marginal = dot(current.reshape(-1, spread), selector, (1,), (0,), BLOCK_PRECISION)
    middle_part = jnp.sum(marginal)
    final_part = jnp.sum(marginal.reshape(per, quarter, 4, 4) * weight)

    sending = current.reshape(per * quarter, -1).T.reshape(devices, -1, LANES)
    lane = jnp.arange(LANES, dtype=jnp.int32)
    extra = jnp.where(lane == 0, middle_part, jnp.where(lane == 1, final_part, 0.0))
    extra = jnp.broadcast_to(extra[None, None, :], (devices, 1, LANES))
    received = lax.all_to_all(jnp.concatenate([sending, extra], axis=1), AXES, 0, 0, tiled=True)
    middle_total = jnp.sum(received[:, -1, 0])
    final_total = jnp.sum(received[:, -1, 1])
    received = received[:, :-1, :]
    current = received.reshape(devices // 4, 4, 8, per, quarter)
    kernel3 = kernel3.reshape(per, devices // 4, spread).transpose(1, 0, 2)
    current = dot(current, kernel3, (0, 3), (0, 1), BLOCK_PRECISION)
    pattern3 = bond3[jnp.arange(8) % 4][:, column // quarter]
    current = current * pattern3[None, :, None, :]
    current = dot(current, kernel4.reshape(4, quarter, spread), (0, 2), (0, 1), BLOCK_PRECISION)
    pattern4 = bond4[column % 4][:, column // quarter]

    middle_mean = middle_total / whole_count
    last_mean = final_total / middle_mean / whole_count
    current = current * pattern4[None, :, :] / (middle_mean * last_mean)
    growth = jnp.log(middle_mean) + jnp.log(last_mean)
    return (current.reshape(-1), growth)


def solution(mesh):
    in_specs = (P(AXES), P())
    out_specs = (P(AXES), P())
    return jax.shard_map(shards, mesh=mesh, in_specs=in_specs, out_specs=out_specs, check_vma=False)
```

```python
import jax
import jax.numpy as jnp
from jax import lax
from jax.sharding import PartitionSpec as P

BLOCK = 4
WINDOWS = 2
AXES = ("lead", "sub")
LANES = 128


def block_kernel(vertical, horizontal, spread):
    position = jnp.arange(spread, dtype=jnp.int32)
    digits = [position // 4 ** (BLOCK - 1 - level) % 4 for level in range(BLOCK)]
    kernel = jnp.ones((spread, spread), jnp.float32)
    for level in range(BLOCK):
        same_spin = (digits[level][:, None] == digits[level][None, :]).astype(jnp.float32)
        kernel = kernel * (1.0 + vertical[level] * same_spin)
    for level in range(1, BLOCK):
        chained = (digits[level - 1] == digits[level]).astype(jnp.float32)
        kernel = kernel * (1.0 + horizontal[level] * chained)[None, :]
    labels = jnp.arange(4, dtype=jnp.int32)
    first_bond = 1.0 + horizontal[0] * (labels[:, None] == labels[None, :]).astype(jnp.float32)
    return (kernel, first_bond)


def dot(lhs, rhs, lhs_dims, rhs_dims, precision=lax.Precision.HIGHEST):
    return lax.dot_general(
        lhs,
        rhs,
        ((lhs_dims, rhs_dims), ((), ())),
        precision=precision,
        preferred_element_type=jnp.float32,
    )


BLOCK_PRECISION = lax.Precision.HIGH


def exchange(rows):
    devices = rows.shape[0]
    shaped = rows.reshape(devices, -1, LANES)
    return lax.all_to_all(shaped, AXES, 0, 0, tiled=True).reshape(devices, -1)


def shards(state, couplings):
    lead_count = lax.axis_size("lead")
    sub_count = lax.axis_size("sub")
    devices = lead_count * sub_count
    me = lax.axis_index("lead") * sub_count + lax.axis_index("sub")
    spread = 4**BLOCK
    quarter = spread // 4
    whole_count = state.shape[0] * devices
    kernels = []
    for block in range(2 * WINDOWS):
        first_site = block * BLOCK
        kernels.append(
            block_kernel(
                couplings[0, first_site : first_site + BLOCK],
                couplings[1, first_site : first_site + BLOCK],
                spread,
            )
        )
    (kernel1, bond1), (kernel2, bond2), (kernel3, bond3), (kernel4, bond4) = kernels
    column = jnp.arange(spread, dtype=jnp.int32)

    sending = jnp.transpose(state.reshape(2, spread, -1, LANES), (3, 0, 2, 1))
    received = lax.all_to_all(sending, AXES, 0, 0, tiled=True)
    kernel1 = kernel1 * bond1[me % 4, column // quarter][None, :]
    current = dot(kernel1, received.reshape(spread, -1, spread), (0,), (0,), BLOCK_PRECISION)
    current = dot(current.reshape(-1, spread), kernel2, (1,), (0,), BLOCK_PRECISION)
    pattern2 = bond2[column % 4][:, column // quarter]
    current = current.reshape(spread, -1, spread) * pattern2[:, None, :]
    current = jnp.transpose(current, (1, 0, 2))

    tail = kernel4.reshape(spread, 4, quarter).sum(axis=2)
    tail = dot(tail, bond4, (1,), (1,))
    gather = bond3[:, column // quarter].T[:, None, :] * tail[:, column % 4].T[:, :, None]
    per = spread // (devices // 4)
    rows = lax.dynamic_slice_in_dim(kernel3.reshape(per, devices // 4, spread), me // 4, 1, axis=1)
    cols = lax.dynamic_slice_in_dim(gather, (me % 4) * quarter, quarter, axis=1)
    weight = dot(rows.reshape(per, spread), cols.reshape(spread, -1), (1,), (0,))
    weight = weight.reshape(per, quarter, 1, 4)
    selector = (column[:, None] % 4 == jnp.arange(4)[None, :]).astype(jnp.float32)
    marginal = dot(current.reshape(-1, spread), selector, (1,), (0,))
    middle_part = jnp.sum(marginal)
    final_part = jnp.sum(marginal.reshape(per, quarter, 4, 4) * weight)

    sending = current.reshape(per * quarter, -1).T.reshape(devices, -1, LANES)
    lane = jnp.arange(LANES, dtype=jnp.int32)
    extra = jnp.where(lane == 0, middle_part, jnp.where(lane == 1, final_part, 0.0))
    extra = jnp.broadcast_to(extra[None, None, :], (devices, 1, LANES))
    received = lax.all_to_all(jnp.concatenate([sending, extra], axis=1), AXES, 0, 0, tiled=True)
    middle_total = jnp.sum(received[:, -1, 0])
    final_total = jnp.sum(received[:, -1, 1])
    received = received[:, :-1, :]
    current = received.reshape(devices // 4, 4, 8, per, quarter)
    kernel3 = kernel3.reshape(per, devices // 4, spread).transpose(1, 0, 2)
    current = dot(current, kernel3, (0, 3), (0, 1), BLOCK_PRECISION)
    pattern3 = bond3[jnp.arange(8) % 4][:, column // quarter]
    current = dot(current, kernel4.reshape(4, quarter, spread), (0, 2), (0, 1), BLOCK_PRECISION)
    pattern4 = bond4[column % 4][:, column // quarter]

    middle_mean = middle_total / whole_count
    last_mean = final_total / middle_mean / whole_count
    current = current * (pattern3[:, :, None] * pattern4[None, :, :]) / (middle_mean * last_mean)
    growth = jnp.log(middle_mean) + jnp.log(last_mean)
    return (current.reshape(-1), growth)


def solution(mesh):
    in_specs = (P(AXES), P())
    out_specs = (P(AXES), P())
    return jax.shard_map(shards, mesh=mesh, in_specs=in_specs, out_specs=out_specs, check_vma=False)
```
